256 devices in a mesh: row: 8 (over x_lo, y), col: 32 (over z, x_hi, core).
Axes of the slice: x: 4 (x_hi: 2, x_lo: 2; x = x_hi * 2 + x_lo), y: 4, z: 8, core: 2. Of those that a mesh axis runs over, the one named last changes fastest.
Arguments:
- a_blocks: float32 [32, 8, 32, 4096], P('col', 'row'), may hold values from -0.25 to 0.25
- a_rows: int32 [32, 8, 32], P('col', 'row'), may hold values from 0 to 32, as said below
- a_slots: int32 [32, 8, 32], P('col', 'row'), may hold values from 0 to 23, as said below
- b_stripes: float32 [192, 64, 1024], P('col', None, 'row'), may hold values from -6 to 6
Outputs:
- product: float32 [65536, 1024], P('col', 'row')
The draws below stay inside these ranges and needn't reach their ends.
Inputs may be any that keep to these rules, and one draw needn't show every extreme that they name: `a_rows`: in each group and panel the used slots (row below 32) come first, in rising order of the pair (row, stripe), no pair twice; the remaining slots hold 32. In every draw one group has all 32 slots of all its panels used; in the others each panel uses between a quarter and five eighths of them. `a_slots`: stripe of each slot within its panel; empty slots hold 0.
All inputs are finite; a program needn't handle non-finite values.
Results may differ from the reference program's by a relative error of at most 0.0003.
Values sent between devices are 32-bit elements; how exact they have to be, the bound alone decides.
No kernel may reach another device: no remote copies, remote signals or barrier semaphores. Data moves between devices by JAX's collectives and lax.ppermute only.
A program may use at most 64 MiB of HBM per device.

```python
import jax
import jax.numpy as jnp
from jax import lax

BLK = 64
MB = 32
CA = 32
SP = 24
STRIPES = 192
COLS = 1024
N_ROW = 8
N_COL = 32


def pattern_pairs(key):
    base = jax.random.fold_in(key, 17)
    key_busy, key_count, key_perm = jax.random.split(base, 3)
    busy = jax.random.randint(key_busy, (), 0, N_COL)
    counts = jax.random.randint(key_count, (N_COL, N_ROW), max(1, CA // 4), CA * 5 // 8 + 1)
    counts = jnp.where(jnp.arange(N_COL)[:, None] == busy, CA, counts)
    total_pairs = MB * SP
    keys = jax.random.split(key_perm, N_COL * N_ROW)
    picks = jax.vmap(lambda k: jax.random.permutation(k, total_pairs)[:CA])(keys)
    picks = picks.reshape(N_COL, N_ROW, CA).astype(jnp.int32)
    used = jnp.arange(CA)[None, None, :] < counts[:, :, None]
    picks = jnp.where(used, picks, total_pairs)
    return jnp.sort(picks, axis=-1)


def draw_a_rows(key, part):
    pairs = pattern_pairs(key)
    return (pairs // SP).astype(jnp.int32)


def draw_a_slots(key, part):
    pairs = pattern_pairs(key)
    return jnp.where(pairs < MB * SP, pairs % SP, 0).astype(jnp.int32)


def steps_of(key, extent, shards, low, high):
    def one(dim, blocks):
        steps = jax.random.uniform(jax.random.fold_in(jax.random.fold_in(key, 6), dim), (blocks,), jnp.float32, low / len(shards), high / len(shards))
        return jnp.repeat(jnp.exp(steps), extent[dim] // blocks).reshape((-1,) + (1,) * (len(extent) - dim - 1))

    factor_of = one(*shards[0])
    for cut in shards[1:]:
        factor_of = factor_of * one(*cut)
    return factor_of


def noise(stream_key, extent, scale, bound, cuts=(), kind=jnp.bfloat16):
    array = jax.random.normal(stream_key, extent, jnp.float32) * scale
    if len(cuts) > 0:
        array = steps_of(stream_key, extent, cuts, -0.22, 0.18) * array
    return jnp.clip(array, min=-bound, max=bound).astype(kind)


def setup_inputs(seed: int = 0) -> dict:
    arg_keys = jax.random.split(jax.random.key(seed), 5)
    return {
        "a_blocks": noise(arg_keys[0], (N_COL, N_ROW, CA, BLK * BLK), (8 * BLK) ** -0.5, 0.25, ((0, 32), (1, 8)), jnp.float32),
        "a_rows": draw_a_rows(jax.random.fold_in(arg_keys[4], 71), 0),
        "a_slots": draw_a_slots(jax.random.fold_in(arg_keys[4], 71), 0),
        "b_stripes": noise(arg_keys[3], (STRIPES, BLK, COLS), 1.0, 6.0, ((0, 32), (2, 8)), jnp.float32),
    }


def reference(a_blocks, a_rows, a_slots, b_stripes):
    n_col, n_row, capacity = a_rows.shape
    panel_slots = b_stripes.shape[0] // n_row
    columns = b_stripes.shape[2]

    def one_group(carry, inputs):
        blocks, rows, slots = inputs

        def one_panel(panel, acc):
            left = blocks[panel].reshape(capacity, BLK, BLK)
            index = (panel * panel_slots + slots[panel]).astype(jnp.int32)
            chosen = jnp.take(b_stripes, index, axis=0)
            terms = jnp.einsum("gij,gjc->gic", left, chosen, precision=lax.Precision.HIGHEST)
            return acc.at[rows[panel]].add(terms)

        start = jnp.zeros((MB + 1, BLK, columns), jnp.float32)
        acc = lax.fori_loop(0, n_row, one_panel, start)
        return carry, acc[:MB]

    _, tiles = lax.scan(one_group, jnp.zeros((), jnp.float32), (a_blocks, a_rows, a_slots))
    return tiles.reshape(n_col * MB * BLK, columns)
```

```python
import jax
import jax.numpy as jnp
from jax import lax
from jax.sharding import Mesh
from jax.sharding import PartitionSpec as P

BLK = 64
MB = 32

AXES = ("xl", "y", "z", "xh", "core")
ROW = ("xl", "y")
COL = ("z", "xh", "core")


def swap(block, axis):
    return lax.ppermute(block, axis, [(0, 1), (1, 0)])


def shift(block, axis, distance):
    n = lax.axis_size(axis)
    return lax.ppermute(block, axis, [(i, (i + distance) % n) for i in range(n)])


def gather_a(a_own):
    n_y = lax.axis_size("y")
    xl = lax.axis_index("xl")
    y = lax.axis_index("y")
    a_x = swap(a_own, "xl")
    bundle = jnp.stack([a_own, a_x])
    from_minus = shift(bundle, "y", 1)
    from_plus = shift(bundle, "y", -1)
    far_a = shift(from_plus[0], "y", -1)
    far_b = shift(from_minus[1], "y", 1)
    panels = [a_own, a_x, from_minus[0], from_minus[1], from_plus[0], from_plus[1], far_a, far_b]
    ys = [y, y, y - 1, y - 1, y + 1, y + 1, y + 2, y + 2]
    xls = [xl, 1 - xl] * 4
    pid = jnp.stack([xls[k] * n_y + (ys[k] % n_y) for k in range(8)]).astype(jnp.int32)
    return jnp.stack(panels), pid


def gather_b(b_own):
    n_z = lax.axis_size("z")
    xh = lax.axis_index("xh")
    core = lax.axis_index("core")
    b_h = swap(b_own, "xh")
    pair = jnp.where(xh == 0, jnp.stack([b_own, b_h]), jnp.stack([b_h, b_own]))
    by_offset = [None] * n_z
    by_offset[0] = pair
    up = pair
    down = pair
    half = n_z // 2
    for d in range(1, half):
        up = shift(up, "z", -1)
        down = shift(down, "z", 1)
        by_offset[d] = up
        by_offset[n_z - d] = down
    far_up = shift(up[0], "z", -1)
    far_down = shift(down[1], "z", 1)
    by_offset[half] = jnp.stack([far_up, far_down])
    mine = jnp.stack(by_offset)
    other = swap(mine, "core")
    return jnp.where(core == 0, jnp.stack([mine, other]), jnp.stack([other, mine]))


def shards(a_blocks, a_rows, a_slots, b_stripes):
    n_z = lax.axis_size("z")
    z = lax.axis_index("z")
    columns = b_stripes.shape[2]
    highest = lax.Precision.HIGHEST

    ints = jnp.stack([a_rows[0, 0], a_slots[0, 0]])
    all_ints = lax.all_gather(ints, ROW, axis=0, tiled=False)

    a_all, pid = gather_a(a_blocks[0, 0])
    table = gather_b(b_stripes)
    table = table.reshape(-1, BLK, columns)

    ints_k = jnp.take(all_ints, pid, axis=0)
    rows = ints_k[:, 0]
    slots = ints_k[:, 1]
    d = (pid[:, None] - z) % n_z
    index = (((slots // 6) % 2 * n_z + d) * 2 + slots // 12) * 6 + slots % 6
    chosen = jnp.take(table, index.reshape(-1), axis=0)
    left = a_all.reshape(-1, BLK, BLK)
    terms = jnp.einsum("gij,gjc->gic", left, chosen, precision=highest)
    place = (rows.reshape(-1)[:, None] == jnp.arange(MB, dtype=jnp.int32)[None, :]).astype(jnp.float32)
    out = jnp.einsum("gm,gic->mic", place, terms, precision=highest)
    return out.reshape(MB * BLK, columns)


def solution(mesh):
    fine = Mesh(mesh.devices.reshape(2, 4, 8, 2, 2), AXES)
    return jax.shard_map(
        shards,
        mesh=fine,
        in_specs=(
            P(COL, ROW, None, None),
            P(COL, ROW, None),
            P(COL, ROW, None),
            P(COL, None, ROW),
        ),
        out_specs=P(COL, ROW),
        check_vma=False,
    )
```

```python
import jax
import jax.numpy as jnp
from jax import lax
from jax.sharding import Mesh
from jax.sharding import PartitionSpec as P

BLK = 64
MB = 32

AXES = ("xl", "y", "z", "xh", "core")
ROW = ("xl", "y")
COL = ("z", "xh", "core")


def swap(block, axis):
    return lax.ppermute(block, axis, [(0, 1), (1, 0)])


def shift(block, axis, distance):
    n = lax.axis_size(axis)
    return lax.ppermute(block, axis, [(i, (i + distance) % n) for i in range(n)])


def as_blocks(panel):
    return panel.reshape(-1, BLK, BLK)


def gather_a(a_own):
    n_y = lax.axis_size("y")
    xl = lax.axis_index("xl")
    y = lax.axis_index("y")
    a_x = swap(a_own, "xl")
    bundle = jnp.stack([a_own, a_x])
    from_minus = shift(bundle, "y", 1)
    from_plus = shift(bundle, "y", -1)
    far_a = shift(from_plus[0], "y", -1)
    far_b = shift(from_minus[1], "y", 1)
    panels = [a_own, a_x, from_minus[0], from_minus[1], from_plus[0], from_plus[1], far_a, far_b]
    ys = [y, y, y - 1, y - 1, y + 1, y + 1, y + 2, y + 2]
    xls = [xl, 1 - xl] * 4
    pid = jnp.stack([xls[k] * n_y + (ys[k] % n_y) for k in range(8)]).astype(jnp.int32)
    return panels, pid


def b_by_offset(b_own):
    n_z = lax.axis_size("z")
    pair = jnp.stack([b_own, swap(b_own, "xh")])
    by_offset = [None] * n_z
    by_offset[0] = pair
    up = pair
    down = pair
    half = n_z // 2
    for d in range(1, half):
        up = shift(up, "z", -1)
        down = shift(down, "z", 1)
        by_offset[d] = up
        by_offset[n_z - d] = down
    far_up = shift(up[0], "z", -1)
    far_down = shift(down[1], "z", 1)
    by_offset[half] = jnp.stack([far_up, far_down])
    return by_offset


def shards(a_blocks, a_rows, a_slots, b_stripes):
    n_z = lax.axis_size("z")
    z = lax.axis_index("z")
    xh = lax.axis_index("xh")
    core = lax.axis_index("core")
    columns = b_stripes.shape[2]

    a_own = a_blocks[0, 0]
    width = a_own.shape[1]
    ints = jnp.stack([a_rows[0, 0], a_slots[0, 0]], axis=1).astype(jnp.float32)
    ints = jnp.pad(ints, ((0, 0), (0, 128 - 2)))
    payloads, pid = gather_a(jnp.concatenate([a_own, ints], axis=1))
    a_all = jnp.stack([as_blocks(q[:, :width]) for q in payloads])
    all_ints = jnp.stack([q[:, width:width + 2] for q in payloads]).astype(jnp.int32)
    position = jnp.argsort(pid).astype(jnp.int32)
    by_offset = b_by_offset(b_stripes)

    out = jnp.zeros((MB, BLK, columns), jnp.float32)
    row_ids = jnp.arange(MB, dtype=jnp.int32)
    for d in range(n_z):
        mine = by_offset[d]
        other = swap(mine, "core")
        table = jnp.stack([mine, other]).reshape(-1, BLK, columns)
        p = (z + d) % n_z
        k = position[p]
        rows = all_ints[k, :, 0]
        slots = all_ints[k, :, 1]
        index = (((slots // 6) % 2 ^ core) * 2 + ((slots // 12) ^ xh)) * 6 + slots % 6
        chosen = jnp.take(table, index, axis=0)
        left = a_all[k]
        terms = jnp.einsum("gij,gjc->gic", left, chosen, precision=lax.Precision.HIGH)
        place = (rows[:, None] == row_ids[None, :]).astype(jnp.float32)
        out = out + jnp.einsum("gm,gic->mic", place, terms, precision=lax.Precision.HIGHEST)
    return out.reshape(MB * BLK, columns)


def solution(mesh):
    fine = Mesh(mesh.devices.reshape(2, 4, 8, 2, 2), AXES)
    return jax.shard_map(
        shards,
        mesh=fine,
        in_specs=(
            P(COL, ROW, None, None),
            P(COL, ROW, None),
            P(COL, ROW, None),
            P(COL, None, ROW),
        ),
        out_specs=P(COL, ROW),
        check_vma=False,
    )
```

```python
import jax
import jax.numpy as jnp
from jax import lax
from jax.sharding import Mesh
from jax.sharding import PartitionSpec as P

BLK = 64
MB = 32

AXES = ("xl", "y", "z", "xh", "core")
ROW = ("xl", "y")
COL = ("z", "xh", "core")


def swap(block, axis):
    return lax.ppermute(block, axis, [(0, 1), (1, 0)])


def shift(block, axis, distance):
    n = lax.axis_size(axis)
    return lax.ppermute(block, axis, [(i, (i + distance) % n) for i in range(n)])


def gather_a(a_own):
    n_y = lax.axis_size("y")
    xl = lax.axis_index("xl")
    y = lax.axis_index("y")
    a_x = swap(a_own, "xl")
    bundle = jnp.stack([a_own, a_x])
    from_minus = shift(bundle, "y", 1)
    from_plus = shift(bundle, "y", -1)
    far_a = shift(from_plus[0], "y", -1)
    far_b = shift(from_minus[1], "y", 1)
    panels = [a_own, a_x, from_minus[0], from_minus[1], from_plus[0], from_plus[1], far_a, far_b]
    ys = [y, y, y - 1, y - 1, y + 1, y + 1, y + 2, y + 2]
    xls = [xl, 1 - xl] * 4
    pid = jnp.stack([xls[k] * n_y + (ys[k] % n_y) for k in range(8)]).astype(jnp.int32)
    return jnp.stack(panels), pid


def gather_b(b_own):
    n_z = lax.axis_size("z")
    pair = jnp.stack([b_own, swap(b_own, "xh")])
    by_offset = [None] * n_z
    by_offset[0] = pair
    up = pair
    down = pair
    half = n_z // 2
    for d in range(1, half):
        up = shift(up, "z", -1)
        down = shift(down, "z", 1)
        by_offset[d] = up
        by_offset[n_z - d] = down
    far_up = shift(up[0], "z", -1)
    far_down = shift(down[1], "z", 1)
    by_offset[half] = jnp.stack([far_up, far_down])
    mine = jnp.stack(by_offset)
    return jnp.stack([mine, swap(mine, "core")])


def shards(a_blocks, a_rows, a_slots, b_stripes):
    n_z = lax.axis_size("z")
    z = lax.axis_index("z")
    columns = b_stripes.shape[2]
    highest = lax.Precision.HIGHEST

    ints = jnp.stack([a_rows[0, 0], a_slots[0, 0]])
    ints_k, _ = gather_a(ints)
    a_all, pid = gather_a(a_blocks[0, 0])
    table = gather_b(b_stripes)
    table = table.reshape(-1, BLK, columns)

    rows = ints_k[:, 0]
    slots = ints_k[:, 1]
    d = (pid[:, None] - z) % n_z
    core_rel = (slots // 6) % 2 ^ lax.axis_index("core")
    xh_rel = (slots // 12) ^ lax.axis_index("xh")
    index = ((core_rel * n_z + d) * 2 + xh_rel) * 6 + slots % 6
    chosen = jnp.take(table, index.reshape(-1), axis=0)
    left = a_all.reshape(-1, BLK, BLK)
    terms = jnp.einsum("gij,gjc->gic", left, chosen, precision=lax.Precision.HIGH)
    place = (rows.reshape(-1)[:, None] == jnp.arange(MB, dtype=jnp.int32)[None, :]).astype(jnp.float32)
    out = jnp.einsum("gm,gic->mic", place, terms, precision=highest)
    return out.reshape(MB * BLK, columns)


def solution(mesh):
    fine = Mesh(mesh.devices.reshape(2, 4, 8, 2, 2), AXES)
    return jax.shard_map(
        shards,
        mesh=fine,
        in_specs=(
            P(COL, ROW, None, None),
            P(COL, ROW, None),
            P(COL, ROW, None),
            P(COL, None, ROW),
        ),
        out_specs=P(COL, ROW),
        check_vma=False,
    )
```

```python
import jax
import jax.numpy as jnp
from jax import lax
from jax.sharding import Mesh
from jax.sharding import PartitionSpec as P

BLK = 64
MB = 32

AXES = ("xl", "y", "z", "xh", "core")
ROW = ("xl", "y")
COL = ("z", "xh", "core")


def swap(block, axis):
    return lax.ppermute(block, axis, [(0, 1), (1, 0)])


def shift(block, axis, distance):
    n = lax.axis_size(axis)
    return lax.ppermute(block, axis, [(i, (i + distance) % n) for i in range(n)])


def gather_a(a_own):
    n_y = lax.axis_size("y")
    xl = lax.axis_index("xl")
    y = lax.axis_index("y")
    a_x = swap(a_own, "xl")
    bundle = jnp.stack([a_own, a_x])
    from_minus = shift(bundle, "y", 1)
    from_plus = shift(bundle, "y", -1)
    far_a = shift(from_plus[0], "y", -1)
    far_b = shift(from_minus[1], "y", 1)
    panels = [a_own, a_x, from_minus[0], from_minus[1], from_plus[0], from_plus[1], far_a, far_b]
    ys = [y, y, y - 1, y - 1, y + 1, y + 1, y + 2, y + 2]
    xls = [xl, 1 - xl] * 4
    pid = jnp.stack([xls[k] * n_y + (ys[k] % n_y) for k in range(8)]).astype(jnp.int32)
    return jnp.stack(panels), pid


def gather_b(b_own):
    mine = lax.all_gather(b_own, ("z", "xh"), axis=0, tiled=True)
    return jnp.stack([mine, swap(mine, "core")])


def shards(a_blocks, a_rows, a_slots, b_stripes):
    n_z = lax.axis_size("z")
    z = lax.axis_index("z")
    columns = b_stripes.shape[2]
    highest = lax.Precision.HIGHEST

    a_own = a_blocks[0, 0]
    width = a_own.shape[1]
    ints = jnp.stack([a_rows[0, 0], a_slots[0, 0]], axis=1).astype(jnp.float32)
    ints = jnp.pad(ints, ((0, 0), (0, 128 - 2)))
    payload, pid = gather_a(jnp.concatenate([a_own, ints], axis=1))
    a_all = payload[:, :, :width]
    ints_k = jnp.swapaxes(payload[:, :, width:width + 2], 1, 2).astype(jnp.int32)
    table = gather_b(b_stripes)
    table = table.reshape(-1, BLK, columns)

    rows = ints_k[:, 0]
    slots = ints_k[:, 1]
    core_rel = (slots // 6) % 2 ^ lax.axis_index("core")
    index = ((core_rel * n_z + pid[:, None]) * 2 + slots // 12) * 6 + slots % 6
    chosen = jnp.take(table, index.reshape(-1), axis=0)
    left = a_all.reshape(-1, BLK, BLK)
    terms = jnp.einsum("gij,gjc->gic", left, chosen, precision=lax.Precision.HIGH)
    place = (rows.reshape(-1)[:, None] == jnp.arange(MB, dtype=jnp.int32)[None, :]).astype(jnp.float32)
    out = jnp.einsum("gm,gic->mic", place, terms, precision=highest)
    return out.reshape(MB * BLK, columns)


def solution(mesh):
    fine = Mesh(mesh.devices.reshape(2, 4, 8, 2, 2), AXES)
    return jax.shard_map(
        shards,
        mesh=fine,
        in_specs=(
            P(COL, ROW, None, None),
            P(COL, ROW, None),
            P(COL, ROW, None),
            P(COL, None, ROW),
        ),
        out_specs=P(COL, ROW),
        check_vma=False,
    )
```

```python
import jax
import jax.numpy as jnp
from jax import lax
from jax.sharding import Mesh
from jax.sharding import PartitionSpec as P

BLK = 64
MB = 32

AXES = ("xl", "y", "z", "xh", "core")
ROW = ("xl", "y")
COL = ("z", "xh", "core")


def swap(block, axis):
    return lax.ppermute(block, axis, [(0, 1), (1, 0)])


def shift(block, axis, distance):
    n = lax.axis_size(axis)
    return lax.ppermute(block, axis, [(i, (i + distance) % n) for i in range(n)])


def gather_a(a_own):
    n_y = lax.axis_size("y")
    xl = lax.axis_index("xl")
    y = lax.axis_index("y")
    a_x = swap(a_own, "xl")
    bundle = jnp.stack([a_own, a_x])
    from_minus = shift(bundle, "y", 1)
    from_plus = shift(bundle, "y", -1)
    far_a = shift(from_plus[0], "y", -1)
    far_b = shift(from_minus[1], "y", 1)
    panels = [a_own, a_x, from_minus[0], from_minus[1], from_plus[0], from_plus[1], far_a, far_b]
    ys = [y, y, y - 1, y - 1, y + 1, y + 1, y + 2, y + 2]
    xls = [xl, 1 - xl] * 4
    pid = jnp.stack([xls[k] * n_y + (ys[k] % n_y) for k in range(8)]).astype(jnp.int32)
    return jnp.stack(panels), pid


def gather_b(b_own):
    n_z = lax.axis_size("z")
    pair = jnp.stack([b_own, swap(b_own, "xh")])
    by_offset = [None] * n_z
    by_offset[0] = pair
    up = pair
    down = pair
    half = n_z // 2
    for d in range(1, half):
        up = shift(up, "z", -1)
        down = shift(down, "z", 1)
        by_offset[d] = up
        by_offset[n_z - d] = down
    far_up = shift(up[0], "z", -1)
    far_down = shift(down[1], "z", 1)
    by_offset[half] = jnp.stack([far_up, far_down])
    return jnp.stack(by_offset + [swap(piece, "core") for piece in by_offset])


def shards(a_blocks, a_rows, a_slots, b_stripes):
    n_z = lax.axis_size("z")
    z = lax.axis_index("z")
    columns = b_stripes.shape[2]

    a_own = a_blocks[0, 0]
    width = a_own.shape[1]
    ints = jnp.stack([a_rows[0, 0], a_slots[0, 0]], axis=1).astype(jnp.float32)
    ints = jnp.pad(ints, ((0, 0), (0, 128 - 2)))
    payload, pid = gather_a(jnp.concatenate([a_own, ints], axis=1))
    a_all = payload[:, :, :width]
    ints_k = jnp.swapaxes(payload[:, :, width:width + 2], 1, 2).astype(jnp.int32)
    table = gather_b(b_stripes)
    table = table.reshape(-1, BLK, columns)

    rows = ints_k[:, 0]
    slots = ints_k[:, 1]
    d = (pid[:, None] - z) % n_z
    core_rel = (slots // 6) % 2 ^ lax.axis_index("core")
    xh_rel = (slots // 12) ^ lax.axis_index("xh")
    index = ((core_rel * n_z + d) * 2 + xh_rel) * 6 + slots % 6
    chosen = jnp.take(table, index.reshape(-1), axis=0)
    left = a_all.reshape(-1, BLK, BLK)
    terms = jnp.einsum("gij,gjc->gic", left, chosen, precision=lax.Precision.HIGH)
    place = (rows.reshape(-1)[:, None] == jnp.arange(MB, dtype=jnp.int32)[None, :]).astype(jnp.float32)
    out = jnp.einsum("gm,gic->mic", place, terms, precision=lax.Precision.HIGH)
    return out.reshape(MB * BLK, columns)


def solution(mesh):
    fine = Mesh(mesh.devices.reshape(2, 4, 8, 2, 2), AXES)
    return jax.shard_map(
        shards,
        mesh=fine,
        in_specs=(
            P(COL, ROW, None, None),
            P(COL, ROW, None),
            P(COL, ROW, None),
            P(COL, None, ROW),
        ),
        out_specs=P(COL, ROW),
        check_vma=False,
    )
```

```python
import jax
import jax.numpy as jnp
from jax import lax
from jax.experimental import pallas as pl
from jax.experimental.pallas import tpu as pltpu
from jax.sharding import Mesh
from jax.sharding import PartitionSpec as P

BLK = 64
MB = 32

AXES = ("xl", "y", "z", "xh", "core")
ROW = ("xl", "y")
COL = ("z", "xh", "core")


def swap(block, axis):
    return lax.ppermute(block, axis, [(0, 1), (1, 0)])


def shift(block, axis, distance):
    n = lax.axis_size(axis)
    return lax.ppermute(block, axis, [(i, (i + distance) % n) for i in range(n)])


def gather_a(a_own):
    n_y = lax.axis_size("y")
    xl = lax.axis_index("xl")
    y = lax.axis_index("y")
    a_x = swap(a_own, "xl")
    bundle = jnp.stack([a_own, a_x])
    from_minus = shift(bundle, "y", 1)
    from_plus = shift(bundle, "y", -1)
    far_a = shift(from_plus[0], "y", -1)
    far_b = shift(from_minus[1], "y", 1)
    panels = [a_own, a_x, from_minus[0], from_minus[1], from_plus[0], from_plus[1], far_a, far_b]
    ys = [y, y, y - 1, y - 1, y + 1, y + 1, y + 2, y + 2]
    xls = [xl, 1 - xl] * 4
    pid = jnp.stack([xls[k] * n_y + (ys[k] % n_y) for k in range(8)]).astype(jnp.int32)
    return jnp.stack(panels), pid


def gather_b(b_own):
    n_z = lax.axis_size("z")
    pair = jnp.stack([b_own, swap(b_own, "xh")])
    by_offset = [None] * n_z
    by_offset[0] = pair
    up = pair
    down = pair
    half = n_z // 2
    for d in range(1, half):
        up = shift(up, "z", -1)
        down = shift(down, "z", 1)
        by_offset[d] = up
        by_offset[n_z - d] = down
    far_up = shift(up[0], "z", -1)
    far_down = shift(down[1], "z", 1)
    by_offset[half] = jnp.stack([far_up, far_down])
    mine = jnp.stack(by_offset)
    return jnp.stack([mine, swap(mine, "core")])


def product_kernel(index_ref, rows_ref, a_ref, table_ref, out_ref):
    out_ref[...] = jnp.zeros_like(out_ref)
    blocks = out_ref.shape[0]

    def one_slot(g, carry):
        row = rows_ref[g]

        @pl.when(row < blocks)
        def _():
            term = jnp.dot(
                a_ref[g],
                table_ref[index_ref[g]],
                precision=lax.Precision.HIGHEST,
                preferred_element_type=jnp.float32,
            )
            out_ref[row] += term

        return carry

    lax.fori_loop(0, a_ref.shape[0], one_slot, 0)


def product(index, rows, left, table):
    slots, blk, _ = left.shape
    columns = table.shape[2]
    vmem = pl.BlockSpec(memory_space=pltpu.VMEM)
    smem = pl.BlockSpec(memory_space=pltpu.SMEM)
    return pl.pallas_call(
        product_kernel,
        out_shape=jax.ShapeDtypeStruct((MB, blk, columns), jnp.float32),
        in_specs=[smem, smem, vmem, vmem],
        out_specs=vmem,
        compiler_params=pltpu.CompilerParams(vmem_limit_bytes=48 * 1024 * 1024),
        cost_estimate=pl.CostEstimate(
            flops=2 * slots * blk * blk * columns,
            bytes_accessed=4 * (left.size + table.size + MB * blk * columns),
            transcendentals=0,
        ),
    )(index, rows, left, table)


def shards(a_blocks, a_rows, a_slots, b_stripes):
    n_z = lax.axis_size("z")
    z = lax.axis_index("z")
    columns = b_stripes.shape[2]

    ints = jnp.stack([a_rows[0, 0], a_slots[0, 0]])
    ints_k, _ = gather_a(ints)
    a_all, pid = gather_a(a_blocks[0, 0])
    table = gather_b(b_stripes)
    table = table.reshape(-1, BLK, columns)

    rows = ints_k[:, 0]
    slots = ints_k[:, 1]
    d = (pid[:, None] - z) % n_z
    core_rel = (slots // 6) % 2 ^ lax.axis_index("core")
    xh_rel = (slots // 12) ^ lax.axis_index("xh")
    index = ((core_rel * n_z + d) * 2 + xh_rel) * 6 + slots % 6
    left = a_all.reshape(-1, BLK, BLK)
    out = product(index.reshape(-1), rows.reshape(-1), left, table)
    return out.reshape(MB * BLK, columns)


def solution(mesh):
    fine = Mesh(mesh.devices.reshape(2, 4, 8, 2, 2), AXES)
    return jax.shard_map(
        shards,
        mesh=fine,
        in_specs=(
            P(COL, ROW, None, None),
            P(COL, ROW, None),
            P(COL, ROW, None),
            P(COL, None, ROW),
        ),
        out_specs=P(COL, ROW),
        check_vma=False,
    )
```

```python
import jax
import jax.numpy as jnp
from jax import lax
from jax.experimental import pallas as pl
from jax.experimental.pallas import tpu as pltpu
from jax.sharding import Mesh
from jax.sharding import PartitionSpec as P

BLK = 64
MB = 32

AXES = ("xl", "y", "z", "xh", "core")
ROW = ("xl", "y")
COL = ("z", "xh", "core")


def swap(block, axis):
    return lax.ppermute(block, axis, [(0, 1), (1, 0)])


def shift(block, axis, distance):
    n = lax.axis_size(axis)
    return lax.ppermute(block, axis, [(i, (i + distance) % n) for i in range(n)])


def gather_a(a_own):
    n_y = lax.axis_size("y")
    xl = lax.axis_index("xl")
    y = lax.axis_index("y")
    a_x = swap(a_own, "xl")
    bundle = jnp.stack([a_own, a_x])
    from_minus = shift(bundle, "y", 1)
    from_plus = shift(bundle, "y", -1)
    far_a = shift(from_plus[0], "y", -1)
    far_b = shift(from_minus[1], "y", 1)
    panels = [a_own, a_x, from_minus[0], from_minus[1], from_plus[0], from_plus[1], far_a, far_b]
    ys = [y, y, y - 1, y - 1, y + 1, y + 1, y + 2, y + 2]
    xls = [xl, 1 - xl] * 4
    pid = jnp.stack([xls[k] * n_y + (ys[k] % n_y) for k in range(8)]).astype(jnp.int32)
    return jnp.stack(panels), pid


def gather_b(b_own):
    n_z = lax.axis_size("z")
    pair = jnp.stack([b_own, swap(b_own, "xh")])
    by_offset = [None] * n_z
    by_offset[0] = pair
    up = pair
    down = pair
    half = n_z // 2
    for d in range(1, half):
        up = shift(up, "z", -1)
        down = shift(down, "z", 1)
        by_offset[d] = up
        by_offset[n_z - d] = down
    far_up = shift(up[0], "z", -1)
    far_down = shift(down[1], "z", 1)
    by_offset[half] = jnp.stack([far_up, far_down])
    mine = jnp.stack(by_offset)
    return jnp.stack([mine, swap(mine, "core")])


def product_kernel(index_ref, rows_ref, a_ref, table_ref, out_ref):
    out_ref[...] = jnp.zeros_like(out_ref)
    blocks = out_ref.shape[0]

    def one_slot(g, carry):
        row = rows_ref[g]

        @pl.when(row < blocks)
        def _():
            left = a_ref[g]
            right = table_ref[index_ref[g]]
            left_hi = left.astype(jnp.bfloat16)
            left_lo = (left - left_hi.astype(jnp.float32)).astype(jnp.bfloat16)
            right_hi = right.astype(jnp.bfloat16)
            right_lo = (right - right_hi.astype(jnp.float32)).astype(jnp.bfloat16)
            term = jnp.dot(left_hi, right_hi, preferred_element_type=jnp.float32)
            term += jnp.dot(left_hi, right_lo, preferred_element_type=jnp.float32)
            term += jnp.dot(left_lo, right_hi, preferred_element_type=jnp.float32)
            out_ref[row] += term

        return carry

    lax.fori_loop(0, a_ref.shape[0], one_slot, 0)


def product(index, rows, left, table):
    slots, blk, _ = left.shape
    columns = table.shape[2]
    vmem = pl.BlockSpec(memory_space=pltpu.VMEM)
    smem = pl.BlockSpec(memory_space=pltpu.SMEM)
    return pl.pallas_call(
        product_kernel,
        out_shape=jax.ShapeDtypeStruct((MB, blk, columns), jnp.float32),
        in_specs=[smem, smem, vmem, vmem],
        out_specs=vmem,
        compiler_params=pltpu.CompilerParams(vmem_limit_bytes=48 * 1024 * 1024),
        cost_estimate=pl.CostEstimate(
            flops=2 * slots * blk * blk * columns,
            bytes_accessed=4 * (left.size + table.size + MB * blk * columns),
            transcendentals=0,
        ),
    )(index, rows, left, table)


def shards(a_blocks, a_rows, a_slots, b_stripes):
    n_z = lax.axis_size("z")
    z = lax.axis_index("z")
    columns = b_stripes.shape[2]

    ints = jnp.stack([a_rows[0, 0], a_slots[0, 0]])
    ints_k, _ = gather_a(ints)
    a_all, pid = gather_a(a_blocks[0, 0])
    table = gather_b(b_stripes)
    table = table.reshape(-1, BLK, columns)

    rows = ints_k[:, 0]
    slots = ints_k[:, 1]
    d = (pid[:, None] - z) % n_z
    core_rel = (slots // 6) % 2 ^ lax.axis_index("core")
    xh_rel = (slots // 12) ^ lax.axis_index("xh")
    index = ((core_rel * n_z + d) * 2 + xh_rel) * 6 + slots % 6
    left = a_all.reshape(-1, BLK, BLK)
    out = product(index.reshape(-1), rows.reshape(-1), left, table)
    return out.reshape(MB * BLK, columns)


def solution(mesh):
    fine = Mesh(mesh.devices.reshape(2, 4, 8, 2, 2), AXES)
    return jax.shard_map(
        shards,
        mesh=fine,
        in_specs=(
            P(COL, ROW, None, None),
            P(COL, ROW, None),
            P(COL, ROW, None),
            P(COL, None, ROW),
        ),
        out_specs=P(COL, ROW),
        check_vma=False,
    )
```

```python
import jax
import jax.numpy as jnp
from jax import lax
from jax.experimental import pallas as pl
from jax.experimental.pallas import tpu as pltpu
from jax.sharding import Mesh
from jax.sharding import PartitionSpec as P

BLK = 64
MB = 32

AXES = ("xl", "y", "z", "xh", "core")
ROW = ("xl", "y")
COL = ("z", "xh", "core")


def swap(block, axis):
    return lax.ppermute(block, axis, [(0, 1), (1, 0)])


def shift(block, axis, distance):
    n = lax.axis_size(axis)
    return lax.ppermute(block, axis, [(i, (i + distance) % n) for i in range(n)])


def gather_a(a_own):
    n_y = lax.axis_size("y")
    xl = lax.axis_index("xl")
    y = lax.axis_index("y")
    a_x = swap(a_own, "xl")
    bundle = jnp.stack([a_own, a_x])
    from_minus = shift(bundle, "y", 1)
    from_plus = shift(bundle, "y", -1)
    far_a = shift(from_plus[0], "y", -1)
    far_b = shift(from_minus[1], "y", 1)
    panels = [a_own, a_x, from_minus[0], from_minus[1], from_plus[0], from_plus[1], far_a, far_b]
    ys = [y, y, y - 1, y - 1, y + 1, y + 1, y + 2, y + 2]
    xls = [xl, 1 - xl] * 4
    pid = jnp.stack([xls[k] * n_y + (ys[k] % n_y) for k in range(8)]).astype(jnp.int32)
    return jnp.stack(panels), pid


def gather_b(b_own):
    n_z = lax.axis_size("z")
    pair = jnp.stack([b_own, swap(b_own, "xh")])
    by_offset = [None] * n_z
    by_offset[0] = pair
    up = pair
    down = pair
    half = n_z // 2
    for d in range(1, half):
        up = shift(up, "z", -1)
        down = shift(down, "z", 1)
        by_offset[d] = up
        by_offset[n_z - d] = down
    far_up = shift(up[0], "z", -1)
    far_down = shift(down[1], "z", 1)
    by_offset[half] = jnp.stack([far_up, far_down])
    mine = jnp.stack(by_offset)
    return jnp.stack([mine, swap(mine, "core")])


def product_kernel(index_ref, rows_ref, a_ref, table_ref, out_ref, acc_ref):
    acc_ref[...] = jnp.zeros_like(acc_ref)
    blocks = out_ref.shape[0]

    def one_slot(g, carry):
        row = jnp.minimum(rows_ref[g], blocks)
        left = a_ref[g]
        right = table_ref[index_ref[g]]
        left_hi = left.astype(jnp.bfloat16)
        left_lo = (left - left_hi.astype(jnp.float32)).astype(jnp.bfloat16)
        right_hi = right.astype(jnp.bfloat16)
        right_lo = (right - right_hi.astype(jnp.float32)).astype(jnp.bfloat16)
        term = jnp.dot(left_hi, right_hi, preferred_element_type=jnp.float32)
        term += jnp.dot(left_hi, right_lo, preferred_element_type=jnp.float32)
        term += jnp.dot(left_lo, right_hi, preferred_element_type=jnp.float32)
        acc_ref[row] += term
        return carry

    lax.fori_loop(0, a_ref.shape[0], one_slot, 0, unroll=8)
    out_ref[...] = acc_ref[:blocks]


def product(index, rows, left, table):
    slots, blk, _ = left.shape
    columns = table.shape[2]
    vmem = pl.BlockSpec(memory_space=pltpu.VMEM)
    smem = pl.BlockSpec(memory_space=pltpu.SMEM)
    return pl.pallas_call(
        product_kernel,
        out_shape=jax.ShapeDtypeStruct((MB, blk, columns), jnp.float32),
        in_specs=[smem, smem, vmem, vmem],
        out_specs=vmem,
        scratch_shapes=[pltpu.VMEM((MB + 1, blk, columns), jnp.float32)],
        compiler_params=pltpu.CompilerParams(vmem_limit_bytes=48 * 1024 * 1024),
        cost_estimate=pl.CostEstimate(
            flops=2 * slots * blk * blk * columns,
            bytes_accessed=4 * (left.size + table.size + MB * blk * columns),
            transcendentals=0,
        ),
    )(index, rows, left, table)


def shards(a_blocks, a_rows, a_slots, b_stripes):
    n_z = lax.axis_size("z")
    z = lax.axis_index("z")
    columns = b_stripes.shape[2]

    ints = jnp.stack([a_rows[0, 0], a_slots[0, 0]])
    ints_k, _ = gather_a(ints)
    a_all, pid = gather_a(a_blocks[0, 0])
    table = gather_b(b_stripes)
    table = table.reshape(-1, BLK, columns)

    rows = ints_k[:, 0]
    slots = ints_k[:, 1]
    d = (pid[:, None] - z) % n_z
    core_rel = (slots // 6) % 2 ^ lax.axis_index("core")
    xh_rel = (slots // 12) ^ lax.axis_index("xh")
    index = ((core_rel * n_z + d) * 2 + xh_rel) * 6 + slots % 6
    left = a_all.reshape(-1, BLK, BLK)
    out = product(index.reshape(-1), rows.reshape(-1), left, table)
    return out.reshape(MB * BLK, columns)


def solution(mesh):
    fine = Mesh(mesh.devices.reshape(2, 4, 8, 2, 2), AXES)
    return jax.shard_map(
        shards,
        mesh=fine,
        in_specs=(
            P(COL, ROW, None, None),
            P(COL, ROW, None),
            P(COL, ROW, None),
            P(COL, None, ROW),
        ),
        out_specs=P(COL, ROW),
        check_vma=False,
    )
```

```python
import jax
import jax.numpy as jnp
from jax import lax
from jax.experimental import pallas as pl
from jax.experimental.pallas import tpu as pltpu
from jax.sharding import Mesh
from jax.sharding import PartitionSpec as P

BLK = 64
MB = 32

AXES = ("xl", "y", "z", "xh", "core")
ROW = ("xl", "y")
COL = ("z", "xh", "core")


def swap(block, axis):
    return lax.ppermute(block, axis, [(0, 1), (1, 0)])


def shift(block, axis, distance):
    n = lax.axis_size(axis)
    return lax.ppermute(block, axis, [(i, (i + distance) % n) for i in range(n)])


def gather_a(a_own, halves=True):
    n_y = lax.axis_size("y")
    xl = lax.axis_index("xl")
    y = lax.axis_index("y")
    half = a_own.shape[0] // 2
    a_x = swap(a_own, "xl")
    own_minus = shift(a_own, "y", 1)
    own_plus = shift(a_own, "y", -1)
    x_minus = shift(a_x, "y", 1)
    x_plus = shift(a_x, "y", -1)
    if halves:
        far_own = jnp.concatenate([shift(own_plus[:half], "y", -1), shift(own_minus[half:], "y", 1)])
        far_x = jnp.concatenate([shift(x_plus[:half], "y", -1), shift(x_minus[half:], "y", 1)])
    else:
        far_own = shift(own_plus, "y", -1)
        far_x = shift(x_plus, "y", -1)
    panels = [a_own, a_x, own_minus, own_plus, x_minus, x_plus, far_own, far_x]
    ys = [y, y, y - 1, y + 1, y - 1, y + 1, y + 2, y + 2]
    xls = [xl, 1 - xl, xl, xl, 1 - xl, 1 - xl, xl, 1 - xl]
    pid = jnp.stack([xls[k] * n_y + (ys[k] % n_y) for k in range(8)]).astype(jnp.int32)
    return panels, pid


def gather_b(b_own):
    n_z = lax.axis_size("z")
    pair = jnp.stack([b_own, swap(b_own, "xh")])
    by_offset = [None] * n_z
    by_offset[0] = pair
    up = pair
    down = pair
    half = n_z // 2
    for d in range(1, half):
        up = shift(up, "z", -1)
        down = shift(down, "z", 1)
        by_offset[d] = up
        by_offset[n_z - d] = down
    far_up = shift(up[0], "z", -1)
    far_down = shift(down[1], "z", 1)
    by_offset[half] = jnp.stack([far_up, far_down])
    mine = jnp.stack(by_offset)
    return mine, swap(mine, "core")


def product_kernel(index_ref, rows_ref, a_ref, mine_ref, other_ref, out_ref, acc_ref):
    acc_ref[...] = jnp.zeros_like(acc_ref)
    blocks = out_ref.shape[0]

    def one_slot(g, carry):
        row = jnp.minimum(rows_ref[g], blocks)
        left = a_ref[g]
        stripes = mine_ref.shape[0]
        index = index_ref[g]
        local = index % stripes
        right = jnp.where(index < stripes, mine_ref[local], other_ref[local])
        left_hi = left.astype(jnp.bfloat16)
        left_lo = (left - left_hi.astype(jnp.float32)).astype(jnp.bfloat16)
        right_hi = right.astype(jnp.bfloat16)
        right_lo = (right - right_hi.astype(jnp.float32)).astype(jnp.bfloat16)
        term = jnp.dot(left_hi, right_hi, preferred_element_type=jnp.float32)
        term += jnp.dot(left_hi, right_lo, preferred_element_type=jnp.float32)
        term += jnp.dot(left_lo, right_hi, preferred_element_type=jnp.float32)
        acc_ref[row] += term
        return carry

    lax.fori_loop(0, a_ref.shape[0], one_slot, 0, unroll=8)
    out_ref[...] = acc_ref[:blocks]


def product(index, rows, left, mine, other):
    slots, blk, _ = left.shape
    columns = mine.shape[2]
    vmem = pl.BlockSpec(memory_space=pltpu.VMEM)
    smem = pl.BlockSpec(memory_space=pltpu.SMEM)
    return pl.pallas_call(
        product_kernel,
        out_shape=jax.ShapeDtypeStruct((MB, blk, columns), jnp.float32),
        in_specs=[smem, smem, vmem, vmem, vmem],
        out_specs=vmem,
        scratch_shapes=[pltpu.VMEM((MB + 1, blk, columns), jnp.float32)],
        compiler_params=pltpu.CompilerParams(vmem_limit_bytes=48 * 1024 * 1024),
        cost_estimate=pl.CostEstimate(
            flops=2 * slots * blk * blk * columns,
            bytes_accessed=4 * (left.size + 2 * mine.size + MB * blk * columns),
            transcendentals=0,
        ),
    )(index, rows, left, mine, other)


def shards(a_blocks, a_rows, a_slots, b_stripes):
    n_z = lax.axis_size("z")
    z = lax.axis_index("z")
    columns = b_stripes.shape[2]

    ints = jnp.stack([a_rows[0, 0], a_slots[0, 0]])
    ints_k, _ = gather_a(ints, halves=False)
    ints_k = jnp.stack(ints_k)
    panels, pid = gather_a(a_blocks[0, 0])
    a_all = jnp.stack([p.reshape(-1, BLK, BLK) for p in panels])
    mine, other = gather_b(b_stripes)
    mine = mine.reshape(-1, BLK, columns)
    other = other.reshape(-1, BLK, columns)

    rows = ints_k[:, 0]
    slots = ints_k[:, 1]
    d = (pid[:, None] - z) % n_z
    core_rel = (slots // 6) % 2 ^ lax.axis_index("core")
    xh_rel = (slots // 12) ^ lax.axis_index("xh")
    index = ((core_rel * n_z + d) * 2 + xh_rel) * 6 + slots % 6
    left = a_all.reshape(-1, BLK, BLK)
    out = product(index.reshape(-1), rows.reshape(-1), left, mine, other)
    return out.reshape(MB * BLK, columns)


def solution(mesh):
    fine = Mesh(mesh.devices.reshape(2, 4, 8, 2, 2), AXES)
    return jax.shard_map(
        shards,
        mesh=fine,
        in_specs=(
            P(COL, ROW, None, None),
            P(COL, ROW, None),
            P(COL, ROW, None),
            P(COL, None, ROW),
        ),
        out_specs=P(COL, ROW),
        check_vma=False,
    )
```

```python
import jax
import jax.numpy as jnp
from jax import lax
from jax.experimental import pallas as pl
from jax.experimental.pallas import tpu as pltpu
from jax.sharding import Mesh
from jax.sharding import PartitionSpec as P

BLK = 64
MB = 32

AXES = ("xl", "y", "z", "xh", "core")
ROW = ("xl", "y")
COL = ("z", "xh", "core")


def swap(block, axis):
    return lax.ppermute(block, axis, [(0, 1), (1, 0)])


def shift(block, axis, distance):
    n = lax.axis_size(axis)
    return lax.ppermute(block, axis, [(i, (i + distance) % n) for i in range(n)])


def gather_a(a_own):
    n_y = lax.axis_size("y")
    xl = lax.axis_index("xl")
    y = lax.axis_index("y")
    a_x = swap(a_own, "xl")
    bundle = jnp.stack([a_own, a_x])
    from_minus = shift(bundle, "y", 1)
    from_plus = shift(bundle, "y", -1)
    far_a = shift(from_plus[0], "y", -1)
    far_b = shift(from_minus[1], "y", 1)
    panels = [a_own, a_x, from_minus[0], from_minus[1], from_plus[0], from_plus[1], far_a, far_b]
    ys = [y, y, y - 1, y - 1, y + 1, y + 1, y + 2, y + 2]
    xls = [xl, 1 - xl] * 4
    pid = jnp.stack([xls[k] * n_y + (ys[k] % n_y) for k in range(8)]).astype(jnp.int32)
    return jnp.stack(panels), pid


def gather_b(b_own):
    n_z = lax.axis_size("z")
    pair = jnp.stack([b_own, swap(b_own, "xh")])
    by_offset = [None] * n_z
    by_offset[0] = pair
    up = pair
    down = pair
    half = n_z // 2
    for d in range(1, half):
        up = shift(up, "z", -1)
        down = shift(down, "z", 1)
        by_offset[d] = up
        by_offset[n_z - d] = down
    far_up = shift(up[0], "z", -1)
    far_down = shift(down[1], "z", 1)
    by_offset[half] = jnp.stack([far_up, far_down])
    mine = jnp.stack(by_offset)
    return mine, swap(mine, "core")


def product_kernel(index_ref, rows_ref, a_ref, mine_ref, other_ref, out_ref, acc_ref):
    acc_ref[...] = jnp.zeros_like(acc_ref)
    blocks = out_ref.shape[0]
    stripes = mine_ref.shape[0]
    blk = a_ref.shape[1]

    def one_pair(t, carry):
        pair = a_ref[t]
        pair_hi = pair.astype(jnp.bfloat16)
        pair_lo = (pair - pair_hi.astype(jnp.float32)).astype(jnp.bfloat16)
        for u in range(2):
            g = 2 * t + u
            row = jnp.minimum(rows_ref[g], blocks)
            index = index_ref[g]
            local = index % stripes
            right = jnp.where(index < stripes, mine_ref[local], other_ref[local])
            right_hi = right.astype(jnp.bfloat16)
            right_lo = (right - right_hi.astype(jnp.float32)).astype(jnp.bfloat16)
            zeros = jnp.zeros_like(right_hi)
            pieces_hi = [right_hi, zeros] if u == 0 else [zeros, right_hi]
            pieces_lo = [right_lo, zeros] if u == 0 else [zeros, right_lo]
            right_hi = jnp.concatenate(pieces_hi, axis=0)
            right_lo = jnp.concatenate(pieces_lo, axis=0)
            term = jnp.dot(pair_hi, right_hi, preferred_element_type=jnp.float32)
            term += jnp.dot(pair_hi, right_lo, preferred_element_type=jnp.float32)
            term += jnp.dot(pair_lo, right_hi, preferred_element_type=jnp.float32)
            acc_ref[row] += term
        return carry

    lax.fori_loop(0, a_ref.shape[0], one_pair, 0, unroll=4)
    out_ref[...] = acc_ref[:blocks]


def product(index, rows, pairs, mine, other):
    n_pairs, blk, _ = pairs.shape
    columns = mine.shape[2]
    vmem = pl.BlockSpec(memory_space=pltpu.VMEM)
    smem = pl.BlockSpec(memory_space=pltpu.SMEM)
    return pl.pallas_call(
        product_kernel,
        out_shape=jax.ShapeDtypeStruct((MB, blk, columns), jnp.float32),
        in_specs=[smem, smem, vmem, vmem, vmem],
        out_specs=vmem,
        scratch_shapes=[pltpu.VMEM((MB + 1, blk, columns), jnp.float32)],
        compiler_params=pltpu.CompilerParams(vmem_limit_bytes=48 * 1024 * 1024),
        cost_estimate=pl.CostEstimate(
            flops=2 * 2 * n_pairs * blk * blk * columns,
            bytes_accessed=4 * (pairs.size + 2 * mine.size + MB * blk * columns),
            transcendentals=0,
        ),
    )(index, rows, pairs, mine, other)


def as_pairs(panel):
    slots = panel.shape[0]
    blocks = panel.reshape(slots // 2, 2, BLK, BLK)
    return jnp.swapaxes(blocks, 1, 2).reshape(slots // 2, BLK, 2 * BLK)


def shards(a_blocks, a_rows, a_slots, b_stripes):
    n_z = lax.axis_size("z")
    z = lax.axis_index("z")
    columns = b_stripes.shape[2]

    ints = jnp.stack([a_rows[0, 0], a_slots[0, 0]])
    ints_k, _ = gather_a(ints)
    a_all, pid = gather_a(as_pairs(a_blocks[0, 0]))
    mine, other = gather_b(b_stripes)
    mine = mine.reshape(-1, BLK, columns)
    other = other.reshape(-1, BLK, columns)

    rows = ints_k[:, 0]
    slots = ints_k[:, 1]
    d = (pid[:, None] - z) % n_z
    core_rel = (slots // 6) % 2 ^ lax.axis_index("core")
    xh_rel = (slots // 12) ^ lax.axis_index("xh")
    index = ((core_rel * n_z + d) * 2 + xh_rel) * 6 + slots % 6
    pairs = a_all.reshape(-1, BLK, 2 * BLK)
    out = product(index.reshape(-1), rows.reshape(-1), pairs, mine, other)
    return out.reshape(MB * BLK, columns)


def solution(mesh):
    fine = Mesh(mesh.devices.reshape(2, 4, 8, 2, 2), AXES)
    return jax.shard_map(
        shards,
        mesh=fine,
        in_specs=(
            P(COL, ROW, None, None),
            P(COL, ROW, None),
            P(COL, ROW, None),
            P(COL, None, ROW),
        ),
        out_specs=P(COL, ROW),
        check_vma=False,
    )
```

```python
import jax
import jax.numpy as jnp
from jax import lax
from jax.experimental import pallas as pl
from jax.experimental.pallas import tpu as pltpu
from jax.sharding import Mesh

from jax.sharding import PartitionSpec as P

BLK = 64
MB = 32

AXES = ("xl", "y", "z", "xh", "core")
ROW = ("xl", "y")
COL = ("z", "xh", "core")


def swap(block, axis):
    return lax.ppermute(block, axis, [(0, 1), (1, 0)])


def shift(block, axis, distance):
    n = lax.axis_size(axis)
    return lax.ppermute(block, axis, [(i, (i + distance) % n) for i in range(n)])


def gather_a(a_own):
    n_y = lax.axis_size("y")
    xl = lax.axis_index("xl")
    y = lax.axis_index("y")
    a_x = swap(a_own, "xl")
    bundle = jnp.stack([a_own, a_x])
    from_minus = shift(bundle, "y", 1)
    from_plus = shift(bundle, "y", -1)
    far_a = shift(from_plus[0], "y", -1)
    far_b = shift(from_minus[1], "y", 1)
    panels = [a_own, a_x, from_minus[0], from_minus[1], from_plus[0], from_plus[1], far_a, far_b]
    ys = [y, y, y - 1, y - 1, y + 1, y + 1, y + 2, y + 2]
    xls = [xl, 1 - xl] * 4
    pid = jnp.stack([xls[k] * n_y + (ys[k] % n_y) for k in range(8)]).astype(jnp.int32)
    return jnp.stack(panels), pid


def gather_b(b_own):
    n_z = lax.axis_size("z")
    pair = jnp.stack([b_own, swap(b_own, "xh")])
    by_offset = [None] * n_z
    by_offset[0] = pair
    up = pair
    down = pair
    half = n_z // 2
    for d in range(1, half):
        up = shift(up, "z", -1)
        down = shift(down, "z", 1)
        by_offset[d] = up
        by_offset[n_z - d] = down
    far_up = shift(up[0], "z", -1)
    far_down = shift(down[1], "z", 1)
    by_offset[half] = jnp.stack([far_up, far_down])
    mine = jnp.stack(by_offset)
    return mine, swap(mine, "core")


def product_kernel(index_ref, rows_ref, a_ref, mine_ref, other_ref, out_ref, acc_ref):
    acc_ref[...] = jnp.zeros_like(acc_ref)
    blocks = out_ref.shape[0]
    stripes = mine_ref.shape[0]

    def one_pair(t, carry):
        pair = a_ref[t]
        pair_hi = pair.astype(jnp.bfloat16)
        pair_lo = (pair - pair_hi.astype(jnp.float32)).astype(jnp.bfloat16)
        for u in range(2):
            g = 2 * t + u
            row = jnp.minimum(rows_ref[g], blocks)
            index = index_ref[g]
            local = index % stripes
            right = jnp.where(index < stripes, mine_ref[local], other_ref[local])
            right_hi = right.astype(jnp.bfloat16)
            right_lo = (right - right_hi.astype(jnp.float32)).astype(jnp.bfloat16)
            zeros = jnp.zeros_like(right_hi)
            pieces_hi = [right_hi, zeros] if u == 0 else [zeros, right_hi]
            pieces_lo = [right_lo, zeros] if u == 0 else [zeros, right_lo]
            right_hi = jnp.concatenate(pieces_hi, axis=0)
            right_lo = jnp.concatenate(pieces_lo, axis=0)
            term = jnp.dot(pair_hi, right_hi, preferred_element_type=jnp.float32)
            term += jnp.dot(pair_hi, right_lo, preferred_element_type=jnp.float32)
            term += jnp.dot(pair_lo, right_hi, preferred_element_type=jnp.float32)
            acc_ref[row] += term
        return carry

    lax.fori_loop(0, a_ref.shape[0], one_pair, 0, unroll=4)
    out_ref[...] = acc_ref[:blocks]


def product(index, rows, pairs, mine, other):
    n_pairs, blk, _ = pairs.shape
    columns = mine.shape[2]
    vmem = pl.BlockSpec(memory_space=pltpu.VMEM)
    smem = pl.BlockSpec(memory_space=pltpu.SMEM)
    return pl.pallas_call(
        product_kernel,
        out_shape=jax.ShapeDtypeStruct((MB, blk, columns), jnp.float32),
        in_specs=[smem, smem, vmem, vmem, vmem],
        out_specs=vmem,
        scratch_shapes=[pltpu.VMEM((MB + 1, blk, columns), jnp.float32)],
        compiler_params=pltpu.CompilerParams(vmem_limit_bytes=48 * 1024 * 1024),
        cost_estimate=pl.CostEstimate(
            flops=2 * 2 * n_pairs * blk * blk * columns,
            bytes_accessed=4 * (pairs.size + 2 * mine.size + MB * blk * columns),
            transcendentals=0,
        ),
    )(index, rows, pairs, mine, other)


def as_pairs(panel):
    slots = panel.shape[0]
    blocks = panel.reshape(slots // 2, 2, BLK, BLK)
    return jnp.swapaxes(blocks, 1, 2).reshape(slots // 2, BLK, 2 * BLK)


def shards_body(a_blocks, a_rows, a_slots, b_stripes):
    n_z = lax.axis_size("z")
    z = lax.axis_index("z")
    columns = b_stripes.shape[2]

    ints = jnp.stack([a_rows[0, 0], a_slots[0, 0]])
    ints_k, _ = gather_a(ints)
    a_all, pid = gather_a(as_pairs(a_blocks[0, 0]))
    mine, other = gather_b(b_stripes)
    mine = mine.reshape(-1, BLK, columns)
    other = other.reshape(-1, BLK, columns)

    rows = ints_k[:, 0]
    slots = ints_k[:, 1]
    d = (pid[:, None] - z) % n_z
    core_rel = (slots // 6) % 2 ^ lax.axis_index("core")
    xh_rel = (slots // 12) ^ lax.axis_index("xh")
    index = ((core_rel * n_z + d) * 2 + xh_rel) * 6 + slots % 6
    pairs = a_all.reshape(-1, BLK, 2 * BLK)
    out = product(index.reshape(-1), rows.reshape(-1), pairs, mine, other)
    return out.reshape(MB * BLK, columns)


def solution(mesh):
    fine = Mesh(mesh.devices.reshape(2, 4, 8, 2, 2), AXES)
    return jax.shard_map(
        shards_body,
        mesh=fine,
        in_specs=(
            P(COL, ROW, None, None),
            P(COL, ROW, None),
            P(COL, ROW, None),
            P(COL, None, ROW),
        ),
        out_specs=P(COL, ROW),
        check_vma=False,
    )
```

```python
import functools

import jax
import jax.numpy as jnp
from jax import lax
from jax.experimental import pallas as pl
from jax.experimental.pallas import tpu as pltpu
from jax.sharding import Mesh

from jax.sharding import PartitionSpec as P

BLK = 64
MB = 32

AXES = ("xl", "y", "z", "xh", "core")
ROW = ("xl", "y")
COL = ("z", "xh", "core")


def swap(block, axis):
    return lax.ppermute(block, axis, [(0, 1), (1, 0)])


def shift(block, axis, distance):
    n = lax.axis_size(axis)
    return lax.ppermute(block, axis, [(i, (i + distance) % n) for i in range(n)])


def gather_a(a_own):
    n_y = lax.axis_size("y")
    xl = lax.axis_index("xl")
    y = lax.axis_index("y")
    a_x = swap(a_own, "xl")
    bundle = jnp.stack([a_own, a_x])
    from_minus = shift(bundle, "y", 1)
    from_plus = shift(bundle, "y", -1)
    far_a = shift(from_plus[0], "y", -1)
    far_b = shift(from_minus[1], "y", 1)
    pieces = [a_own[None], a_x[None], from_minus, from_plus, far_a[None], far_b[None]]
    ys = [y, y, y - 1, y - 1, y + 1, y + 1, y + 2, y + 2]
    xls = [xl, 1 - xl] * 4
    pid = jnp.stack([xls[k] * n_y + (ys[k] % n_y) for k in range(8)]).astype(jnp.int32)
    return pieces, pid


def gather_b(b_own):
    n_z = lax.axis_size("z")
    pair = jnp.stack([b_own, swap(b_own, "xh")])
    by_offset = [None] * n_z
    by_offset[0] = pair
    up = pair
    down = pair
    half = n_z // 2
    for d in range(1, half):
        up = shift(up, "z", -1)
        down = shift(down, "z", 1)
        by_offset[d] = up
        by_offset[n_z - d] = down
    far_up = shift(up[0], "z", -1)
    far_down = shift(down[1], "z", 1)
    by_offset[half] = jnp.stack([far_up, far_down])
    mine = jnp.stack(by_offset)
    other = jnp.stack([swap(piece, "core") for piece in by_offset])
    return mine, other


def product_kernel(n_pieces, index_ref, rows_ref, *refs):
    a_refs = refs[:n_pieces]
    mine_ref, other_ref, out_ref, acc_ref = refs[n_pieces:]
    acc_ref[...] = jnp.zeros_like(acc_ref)
    blocks = out_ref.shape[0]
    stripes = mine_ref.shape[0]

    panel = 0
    for a_ref in a_refs:
        for j in range(a_ref.shape[0]):
            n_pairs = a_ref.shape[1]
            base = panel * 2 * n_pairs

            def one_pair(t, carry, a_ref=a_ref, j=j, base=base):
                pair = a_ref[j, t]
                pair_hi = pair.astype(jnp.bfloat16)
                pair_lo = (pair - pair_hi.astype(jnp.float32)).astype(jnp.bfloat16)
                for u in range(2):
                    g = base + 2 * t + u
                    row = jnp.minimum(rows_ref[g], blocks)
                    index = index_ref[g]
                    local = index % stripes
                    right = jnp.where(index < stripes, mine_ref[local], other_ref[local])
                    right_hi = right.astype(jnp.bfloat16)
                    right_lo = (right - right_hi.astype(jnp.float32)).astype(jnp.bfloat16)
                    zeros = jnp.zeros_like(right_hi)
                    pieces_hi = [right_hi, zeros] if u == 0 else [zeros, right_hi]
                    pieces_lo = [right_lo, zeros] if u == 0 else [zeros, right_lo]
                    right_hi = jnp.concatenate(pieces_hi, axis=0)
                    right_lo = jnp.concatenate(pieces_lo, axis=0)
                    term = jnp.dot(pair_hi, right_hi, preferred_element_type=jnp.float32)
                    term += jnp.dot(pair_hi, right_lo, preferred_element_type=jnp.float32)
                    term += jnp.dot(pair_lo, right_hi, preferred_element_type=jnp.float32)
                    acc_ref[row] += term
                return carry

            lax.fori_loop(0, n_pairs, one_pair, 0, unroll=4)
            panel += 1
    out_ref[...] = acc_ref[:blocks]


def product(index, rows, pieces, mine, other):
    _, n_pairs, blk, _ = pieces[0].shape
    n_panels = sum(piece.shape[0] for piece in pieces)
    columns = mine.shape[2]
    vmem = pl.BlockSpec(memory_space=pltpu.VMEM)
    smem = pl.BlockSpec(memory_space=pltpu.SMEM)
    return pl.pallas_call(
        functools.partial(product_kernel, len(pieces)),
        out_shape=jax.ShapeDtypeStruct((MB, blk, columns), jnp.float32),
        in_specs=[smem, smem] + [vmem] * (len(pieces) + 2),
        out_specs=vmem,
        scratch_shapes=[pltpu.VMEM((MB + 1, blk, columns), jnp.float32)],
        compiler_params=pltpu.CompilerParams(vmem_limit_bytes=48 * 1024 * 1024),
        cost_estimate=pl.CostEstimate(
            flops=2 * 2 * n_panels * n_pairs * blk * blk * columns,
            bytes_accessed=4 * (sum(piece.size for piece in pieces) + 2 * mine.size + MB * blk * columns),
            transcendentals=0,
        ),
    )(index, rows, *pieces, mine, other)


def as_pairs(panel):
    slots = panel.shape[0]
    blocks = panel.reshape(slots // 2, 2, BLK, BLK)
    return jnp.swapaxes(blocks, 1, 2).reshape(slots // 2, BLK, 2 * BLK)


def shards_body(a_blocks, a_rows, a_slots, b_stripes):
    n_z = lax.axis_size("z")
    z = lax.axis_index("z")
    columns = b_stripes.shape[2]

    ints = jnp.stack([a_rows[0, 0], a_slots[0, 0]])
    ints_k, _ = gather_a(ints)
    ints_k = jnp.concatenate(ints_k)
    a_pieces, pid = gather_a(as_pairs(a_blocks[0, 0]))
    mine, other = gather_b(b_stripes)
    mine = mine.reshape(-1, BLK, columns)
    other = other.reshape(-1, BLK, columns)

    rows = ints_k[:, 0]
    slots = ints_k[:, 1]
    d = (pid[:, None] - z) % n_z
    core_rel = (slots // 6) % 2 ^ lax.axis_index("core")
    xh_rel = (slots // 12) ^ lax.axis_index("xh")
    index = ((core_rel * n_z + d) * 2 + xh_rel) * 6 + slots % 6
    out = product(index.reshape(-1), rows.reshape(-1), a_pieces, mine, other)
    return out.reshape(MB * BLK, columns)


def solution(mesh):
    fine = Mesh(mesh.devices.reshape(2, 4, 8, 2, 2), AXES)
    return jax.shard_map(
        shards_body,
        mesh=fine,
        in_specs=(
            P(COL, ROW, None, None),
            P(COL, ROW, None),
            P(COL, ROW, None),
            P(COL, None, ROW),
        ),
        out_specs=P(COL, ROW),
        check_vma=False,
    )
```

```python
import functools

import jax
import jax.numpy as jnp
from jax import lax
from jax.experimental import pallas as pl
from jax.experimental.pallas import tpu as pltpu
from jax.sharding import Mesh

from jax.sharding import PartitionSpec as P

BLK = 64
MB = 32

AXES = ("xl", "y", "z", "xh", "core")
ROW = ("xl", "y")
COL = ("z", "xh", "core")


def swap(block, axis):
    return lax.ppermute(block, axis, [(0, 1), (1, 0)])


def shift(block, axis, distance):
    n = lax.axis_size(axis)
    return lax.ppermute(block, axis, [(i, (i + distance) % n) for i in range(n)])


def gather_a(a_own):
    n_y = lax.axis_size("y")
    xl = lax.axis_index("xl")
    y = lax.axis_index("y")
    a_x = swap(a_own, "xl")
    bundle = jnp.stack([a_own, a_x])
    from_minus = shift(bundle, "y", 1)
    from_plus = shift(bundle, "y", -1)
    far_a = shift(from_plus[0], "y", -1)
    far_b = shift(from_minus[1], "y", 1)
    pieces = [a_own[None], a_x[None], from_minus, from_plus, far_a[None], far_b[None]]
    ys = [y, y, y - 1, y - 1, y + 1, y + 1, y + 2, y + 2]
    xls = [xl, 1 - xl] * 4
    pid = jnp.stack([xls[k] * n_y + (ys[k] % n_y) for k in range(8)]).astype(jnp.int32)
    return pieces, pid


def gather_b(b_own):
    n_z = lax.axis_size("z")
    pair = jnp.stack([b_own, swap(b_own, "xh")])
    by_offset = [None] * n_z
    by_offset[0] = pair
    up = pair
    down = pair
    half = n_z // 2
    for d in range(1, half):
        up = shift(up, "z", -1)
        down = shift(down, "z", 1)
        by_offset[d] = up
        by_offset[n_z - d] = down
    far_up = shift(up[0], "z", -1)
    far_down = shift(down[1], "z", 1)
    by_offset[half] = jnp.stack([far_up, far_down])
    mine = jnp.stack(by_offset)
    return mine, swap(mine, "core")


def product_kernel(n_pieces, index_ref, rows_ref, *refs):
    a_refs = refs[:n_pieces]
    mine_ref, other_ref, out_ref, acc_ref = refs[n_pieces:]
    acc_ref[...] = jnp.zeros_like(acc_ref)
    blocks = out_ref.shape[0]
    stripes = mine_ref.shape[0]

    panel = 0
    for a_ref in a_refs:
        for j in range(a_ref.shape[0]):
            n_pairs = a_ref.shape[1]
            base = panel * 2 * n_pairs

            def one_pair(t, carry, a_ref=a_ref, j=j, base=base):
                pair = a_ref[j, t]
                pair_hi = pair.astype(jnp.bfloat16)
                pair_lo = (pair - pair_hi.astype(jnp.float32)).astype(jnp.bfloat16)
                both = jnp.concatenate([pair_hi, pair_lo], axis=0)
                rows_a = pair.shape[0]
                targets = []
                halves_hi = []
                halves_lo = []
                for u in range(2):
                    g = base + 2 * t + u
                    targets.append(jnp.minimum(rows_ref[g], blocks))
                    index = index_ref[g]
                    local = index % stripes
                    right = jnp.where(index < stripes, mine_ref[local], other_ref[local])
                    right_hi = right.astype(jnp.bfloat16)
                    right_lo = (right - right_hi.astype(jnp.float32)).astype(jnp.bfloat16)
                    zeros = jnp.zeros_like(right_hi)
                    halves_hi.append(jnp.concatenate([right_hi, zeros] if u == 0 else [zeros, right_hi], axis=0))
                    halves_lo.append(jnp.concatenate([right_lo, zeros] if u == 0 else [zeros, right_lo], axis=0))
                diag_hi = jnp.concatenate(halves_hi, axis=1)
                diag_lo = jnp.concatenate(halves_lo, axis=1)
                with_hi = jnp.dot(both, diag_hi, preferred_element_type=jnp.float32)
                with_lo = jnp.dot(pair_hi, diag_lo, preferred_element_type=jnp.float32)
                columns = mine_ref.shape[2]
                for u in range(2):
                    cols = slice(u * columns, (u + 1) * columns)
                    term = with_hi[:rows_a, cols]
                    term += with_lo[:, cols]
                    term += with_hi[rows_a:, cols]
                    acc_ref[targets[u]] += term
                return carry

            lax.fori_loop(0, n_pairs, one_pair, 0, unroll=4)
            panel += 1
    out_ref[...] = acc_ref[:blocks]


def product(index, rows, pieces, mine, other):
    _, n_pairs, blk, _ = pieces[0].shape
    n_panels = sum(piece.shape[0] for piece in pieces)
    columns = mine.shape[2]
    vmem = pl.BlockSpec(memory_space=pltpu.VMEM)
    smem = pl.BlockSpec(memory_space=pltpu.SMEM)
    return pl.pallas_call(
        functools.partial(product_kernel, len(pieces)),
        out_shape=jax.ShapeDtypeStruct((MB, blk, columns), jnp.float32),
        in_specs=[smem, smem] + [vmem] * (len(pieces) + 2),
        out_specs=vmem,
        scratch_shapes=[pltpu.VMEM((MB + 1, blk, columns), jnp.float32)],
        compiler_params=pltpu.CompilerParams(vmem_limit_bytes=48 * 1024 * 1024),
        cost_estimate=pl.CostEstimate(
            flops=2 * 2 * n_panels * n_pairs * blk * blk * columns,
            bytes_accessed=4 * (sum(piece.size for piece in pieces) + 2 * mine.size + MB * blk * columns),
            transcendentals=0,
        ),
    )(index, rows, *pieces, mine, other)


def as_pairs(panel):
    slots = panel.shape[0]
    blocks = panel.reshape(slots // 2, 2, BLK, BLK)
    return jnp.swapaxes(blocks, 1, 2).reshape(slots // 2, BLK, 2 * BLK)


def shards_body(a_blocks, a_rows, a_slots, b_stripes):
    n_z = lax.axis_size("z")
    z = lax.axis_index("z")
    columns = b_stripes.shape[2]

    ints = jnp.stack([a_rows[0, 0], a_slots[0, 0]])
    ints_k, _ = gather_a(ints)
    ints_k = jnp.concatenate(ints_k)
    a_pieces, pid = gather_a(as_pairs(a_blocks[0, 0]))
    mine, other = gather_b(b_stripes)
    mine = mine.reshape(-1, BLK, columns)
    other = other.reshape(-1, BLK, columns)

    rows = ints_k[:, 0]
    slots = ints_k[:, 1]
    d = (pid[:, None] - z) % n_z
    core_rel = (slots // 6) % 2 ^ lax.axis_index("core")
    xh_rel = (slots // 12) ^ lax.axis_index("xh")
    index = ((core_rel * n_z + d) * 2 + xh_rel) * 6 + slots % 6
    out = product(index.reshape(-1), rows.reshape(-1), a_pieces, mine, other)
    return out.reshape(MB * BLK, columns)


def solution(mesh):
    fine = Mesh(mesh.devices.reshape(2, 4, 8, 2, 2), AXES)
    return jax.shard_map(
        shards_body,
        mesh=fine,
        in_specs=(
            P(COL, ROW, None, None),
            P(COL, ROW, None),
            P(COL, ROW, None),
            P(COL, None, ROW),
        ),
        out_specs=P(COL, ROW),
        check_vma=False,
    )
```

```python
import functools

import jax
import jax.numpy as jnp
from jax import lax
from jax.experimental import pallas as pl
from jax.experimental.pallas import tpu as pltpu
from jax.sharding import Mesh

from jax.sharding import PartitionSpec as P

BLK = 64
MB = 32

AXES = ("xl", "y", "z", "xh", "core")
ROW = ("xl", "y")
COL = ("z", "xh", "core")


def swap(block, axis):
    return lax.ppermute(block, axis, [(0, 1), (1, 0)])


def shift(block, axis, distance):
    n = lax.axis_size(axis)
    return lax.ppermute(block, axis, [(i, (i + distance) % n) for i in range(n)])


def gather_a(a_own):
    n_y = lax.axis_size("y")
    xl = lax.axis_index("xl")
    y = lax.axis_index("y")
    a_x = swap(a_own, "xl")
    bundle = jnp.stack([a_own, a_x])
    from_minus = shift(bundle, "y", 1)
    from_plus = shift(bundle, "y", -1)
    far_a = shift(from_plus[0], "y", -1)
    far_b = shift(from_minus[1], "y", 1)
    pieces = [a_own[None], a_x[None], from_minus, from_plus, far_a[None], far_b[None]]
    ys = [y, y, y - 1, y - 1, y + 1, y + 1, y + 2, y + 2]
    xls = [xl, 1 - xl] * 4
    pid = jnp.stack([xls[k] * n_y + (ys[k] % n_y) for k in range(8)]).astype(jnp.int32)
    return pieces, pid


def gather_b(b_own):
    n_z = lax.axis_size("z")
    pair = jnp.stack([b_own, swap(b_own, "xh")])
    by_offset = [None] * n_z
    by_offset[0] = pair
    up = pair
    down = pair
    half = n_z // 2
    for d in range(1, half):
        up = shift(up, "z", -1)
        down = shift(down, "z", 1)
        by_offset[d] = up
        by_offset[n_z - d] = down
    far_up = shift(up[0], "z", -1)
    far_down = shift(down[1], "z", 1)
    by_offset[half] = jnp.stack([far_up, far_down])
    mine = jnp.stack(by_offset)
    early = jnp.stack(by_offset[:half] + by_offset[half + 1:])
    return mine, swap(early, "core"), swap(by_offset[half], "core")


def product_kernel(n_pieces, index_ref, rows_ref, *refs):
    a_refs = refs[:n_pieces]
    mine_ref, early_ref, late_ref, out_ref, acc_ref = refs[n_pieces:]
    acc_ref[...] = jnp.zeros_like(acc_ref)
    blocks = out_ref.shape[0]
    stripes = mine_ref.shape[0]

    panel = 0
    for a_ref in a_refs:
        for j in range(a_ref.shape[0]):
            n_pairs = a_ref.shape[1]
            base = panel * 2 * n_pairs

            def one_pair(t, carry, a_ref=a_ref, j=j, base=base):
                pair = a_ref[j, t]
                pair_hi = pair.astype(jnp.bfloat16)
                pair_lo = (pair - pair_hi.astype(jnp.float32)).astype(jnp.bfloat16)
                both = jnp.concatenate([pair_hi, pair_lo], axis=0)
                rows_a = pair.shape[0]
                for u in range(2):
                    g = base + 2 * t + u
                    row = jnp.minimum(rows_ref[g], blocks)
                    index = index_ref[g]
                    n_early = early_ref.shape[0]
                    first = jnp.minimum(index, stripes - 1)
                    second = jnp.clip(index - stripes, 0, n_early - 1)
                    third = jnp.clip(index - stripes - n_early, 0, late_ref.shape[0] - 1)
                    right = jnp.where(
                        index < stripes,
                        mine_ref[first],
                        jnp.where(index < stripes + n_early, early_ref[second], late_ref[third]),
                    )
                    right_hi = right.astype(jnp.bfloat16)
                    right_lo = (right - right_hi.astype(jnp.float32)).astype(jnp.bfloat16)
                    zeros = jnp.zeros_like(right_hi)
                    pieces_hi = [right_hi, zeros] if u == 0 else [zeros, right_hi]
                    pieces_lo = [right_lo, zeros] if u == 0 else [zeros, right_lo]
                    right_hi = jnp.concatenate(pieces_hi, axis=0)
                    right_lo = jnp.concatenate(pieces_lo, axis=0)
                    with_hi = jnp.dot(both, right_hi, preferred_element_type=jnp.float32)
                    term = with_hi[:rows_a]
                    term += jnp.dot(pair_hi, right_lo, preferred_element_type=jnp.float32)
                    term += with_hi[rows_a:]
                    acc_ref[row] += term
                return carry

            lax.fori_loop(0, n_pairs, one_pair, 0, unroll=4)
            panel += 1
    out_ref[...] = acc_ref[:blocks]


def product(index, rows, pieces, mine, early, late):
    _, n_pairs, blk, _ = pieces[0].shape
    n_panels = sum(piece.shape[0] for piece in pieces)
    columns = mine.shape[2]
    vmem = pl.BlockSpec(memory_space=pltpu.VMEM)
    smem = pl.BlockSpec(memory_space=pltpu.SMEM)
    return pl.pallas_call(
        functools.partial(product_kernel, len(pieces)),
        out_shape=jax.ShapeDtypeStruct((MB, blk, columns), jnp.float32),
        in_specs=[smem, smem] + [vmem] * (len(pieces) + 3),
        out_specs=vmem,
        scratch_shapes=[pltpu.VMEM((MB + 1, blk, columns), jnp.float32)],
        compiler_params=pltpu.CompilerParams(vmem_limit_bytes=48 * 1024 * 1024),
        cost_estimate=pl.CostEstimate(
            flops=2 * 2 * n_panels * n_pairs * blk * blk * columns,
            bytes_accessed=4 * (sum(piece.size for piece in pieces) + mine.size + early.size + late.size + MB * blk * columns),
            transcendentals=0,
        ),
    )(index, rows, *pieces, mine, early, late)


def as_pairs(panel):
    slots = panel.shape[0]
    blocks = panel.reshape(slots // 2, 2, BLK, BLK)
    return jnp.swapaxes(blocks, 1, 2).reshape(slots // 2, BLK, 2 * BLK)


def shards_body(a_blocks, a_rows, a_slots, b_stripes):
    n_z = lax.axis_size("z")
    z = lax.axis_index("z")
    columns = b_stripes.shape[2]

    ints = jnp.stack([a_rows[0, 0], a_slots[0, 0]])
    ints_k, _ = gather_a(ints)
    ints_k = jnp.concatenate(ints_k)
    a_pieces, pid = gather_a(as_pairs(a_blocks[0, 0]))
    mine, early, late = gather_b(b_stripes)
    mine = mine.reshape(-1, BLK, columns)
    early = early.reshape(-1, BLK, columns)
    late = late.reshape(-1, BLK, columns)

    rows = ints_k[:, 0]
    slots = ints_k[:, 1]
    d = (pid[:, None] - z) % n_z
    core_rel = (slots // 6) % 2 ^ lax.axis_index("core")
    xh_rel = (slots // 12) ^ lax.axis_index("xh")
    half = n_z // 2
    d_other = jnp.where(d < half, d, jnp.where(d > half, d - 1, n_z - 1))
    index = ((core_rel * n_z + jnp.where(core_rel == 1, d_other, d)) * 2 + xh_rel) * 6 + slots % 6
    out = product(index.reshape(-1), rows.reshape(-1), a_pieces, mine, early, late)
    return out.reshape(MB * BLK, columns)


def solution(mesh):
    fine = Mesh(mesh.devices.reshape(2, 4, 8, 2, 2), AXES)
    return jax.shard_map(
        shards_body,
        mesh=fine,
        in_specs=(
            P(COL, ROW, None, None),
            P(COL, ROW, None),
            P(COL, ROW, None),
            P(COL, None, ROW),
        ),
        out_specs=P(COL, ROW),
        check_vma=False,
    )
```

```python
import functools

import jax
import jax.numpy as jnp
from jax import lax
from jax.experimental import pallas as pl
from jax.experimental.pallas import tpu as pltpu
from jax.sharding import Mesh

from jax.sharding import PartitionSpec as P

BLK = 64
MB = 32

AXES = ("xl", "y", "z", "xh", "core")
ROW = ("xl", "y")
COL = ("z", "xh", "core")


def swap(block, axis):
    return lax.ppermute(block, axis, [(0, 1), (1, 0)])


def shift(block, axis, distance):
    n = lax.axis_size(axis)
    return lax.ppermute(block, axis, [(i, (i + distance) % n) for i in range(n)])


def gather_a(a_own):
    n_y = lax.axis_size("y")
    xl = lax.axis_index("xl")
    y = lax.axis_index("y")
    a_x = swap(a_own, "xl")
    bundle = jnp.stack([a_own, a_x])
    from_minus = shift(bundle, "y", 1)
    from_plus = shift(bundle, "y", -1)
    far_a = shift(from_plus[0], "y", -1)
    far_b = shift(from_minus[1], "y", 1)
    pieces = [a_own[None], a_x[None], from_minus, from_plus, far_a[None], far_b[None]]
    ys = [y, y, y - 1, y - 1, y + 1, y + 1, y + 2, y + 2]
    xls = [xl, 1 - xl] * 4
    pid = jnp.stack([xls[k] * n_y + (ys[k] % n_y) for k in range(8)]).astype(jnp.int32)
    return pieces, pid


def gather_b(b_own):
    n_z = lax.axis_size("z")
    pair = jnp.stack([b_own, swap(b_own, "xh")])
    by_offset = [None] * n_z
    by_offset[0] = pair
    up = pair
    down = pair
    half = n_z // 2
    for d in range(1, half):
        up = shift(up, "z", -1)
        down = shift(down, "z", 1)
        by_offset[d] = up
        by_offset[n_z - d] = down
    far_up = shift(up[0], "z", -1)
    far_down = shift(down[1], "z", 1)
    by_offset[half] = jnp.stack([far_up, far_down])
    mine = jnp.stack(by_offset)
    return mine, swap(mine, "core")


def product_kernel(n_pieces, index_ref, rows_ref, *refs):
    a_refs = refs[:n_pieces]
    mine_ref, other_ref, out_ref, acc_ref = refs[n_pieces:]
    acc_ref[...] = jnp.zeros_like(acc_ref)
    blocks = out_ref.shape[0]
    stripes = mine_ref.shape[0]

    panel = 0
    for a_ref in a_refs:
        for j in range(a_ref.shape[0]):
            n_pairs = a_ref.shape[1]
            base = panel * 2 * n_pairs

            def one_pair(t, carry, a_ref=a_ref, j=j, base=base):
                pair = a_ref[j, t]
                pair_hi = pair.astype(jnp.bfloat16)
                pair_lo = (pair - pair_hi.astype(jnp.float32)).astype(jnp.bfloat16)
                both = jnp.concatenate([pair_hi, pair_lo], axis=0)
                rows_a = pair.shape[0]
                for u in range(2):
                    g = base + 2 * t + u
                    row = jnp.minimum(rows_ref[g], blocks)
                    index = index_ref[g]
                    local = index % stripes
                    right = jnp.where(index < stripes, mine_ref[local], other_ref[local])
                    right_hi = right.astype(jnp.bfloat16)
                    right_lo = (right - right_hi.astype(jnp.float32)).astype(jnp.bfloat16)
                    zeros = jnp.zeros_like(right_hi)
                    pieces_hi = [right_hi, zeros] if u == 0 else [zeros, right_hi]
                    pieces_lo = [right_lo, zeros] if u == 0 else [zeros, right_lo]
                    right_hi = jnp.concatenate(pieces_hi, axis=0)
                    right_lo = jnp.concatenate(pieces_lo, axis=0)
                    with_hi = jnp.dot(both, right_hi, preferred_element_type=jnp.float32)
                    term = with_hi[:rows_a]
                    term += jnp.dot(pair_hi, right_lo, preferred_element_type=jnp.float32)
                    term += with_hi[rows_a:]
                    acc_ref[row] += term
                return carry

            lax.fori_loop(0, n_pairs, one_pair, 0, unroll=16)
            panel += 1
    out_ref[...] = acc_ref[:blocks]


def product(index, rows, pieces, mine, other):
    _, n_pairs, blk, _ = pieces[0].shape
    n_panels = sum(piece.shape[0] for piece in pieces)
    columns = mine.shape[2]
    vmem = pl.BlockSpec(memory_space=pltpu.VMEM)
    smem = pl.BlockSpec(memory_space=pltpu.SMEM)
    return pl.pallas_call(
        functools.partial(product_kernel, len(pieces)),
        out_shape=jax.ShapeDtypeStruct((MB, blk, columns), jnp.float32),
        in_specs=[smem, smem] + [vmem] * (len(pieces) + 2),
        out_specs=vmem,
        scratch_shapes=[pltpu.VMEM((MB + 1, blk, columns), jnp.float32)],
        compiler_params=pltpu.CompilerParams(vmem_limit_bytes=48 * 1024 * 1024),
        cost_estimate=pl.CostEstimate(
            flops=2 * 2 * n_panels * n_pairs * blk * blk * columns,
            bytes_accessed=4 * (sum(piece.size for piece in pieces) + 2 * mine.size + MB * blk * columns),
            transcendentals=0,
        ),
    )(index, rows, *pieces, mine, other)


def as_pairs(panel):
    slots = panel.shape[0]
    blocks = panel.reshape(slots // 2, 2, BLK, BLK)
    return jnp.swapaxes(blocks, 1, 2).reshape(slots // 2, BLK, 2 * BLK)


def shards_body(a_blocks, a_rows, a_slots, b_stripes):
    n_z = lax.axis_size("z")
    z = lax.axis_index("z")
    columns = b_stripes.shape[2]

    ints = jnp.stack([a_rows[0, 0], a_slots[0, 0]])
    ints_k, _ = gather_a(ints)
    ints_k = jnp.concatenate(ints_k)
    a_pieces, pid = gather_a(as_pairs(a_blocks[0, 0]))
    mine, other = gather_b(b_stripes)
    mine = mine.reshape(-1, BLK, columns)
    other = other.reshape(-1, BLK, columns)

    rows = ints_k[:, 0]
    slots = ints_k[:, 1]
    d = (pid[:, None] - z) % n_z
    core_rel = (slots // 6) % 2 ^ lax.axis_index("core")
    xh_rel = (slots // 12) ^ lax.axis_index("xh")
    index = ((core_rel * n_z + d) * 2 + xh_rel) * 6 + slots % 6
    out = product(index.reshape(-1), rows.reshape(-1), a_pieces, mine, other)
    return out.reshape(MB * BLK, columns)


def solution(mesh):
    fine = Mesh(mesh.devices.reshape(2, 4, 8, 2, 2), AXES)
    return jax.shard_map(
        shards_body,
        mesh=fine,
        in_specs=(
            P(COL, ROW, None, None),
            P(COL, ROW, None),
            P(COL, ROW, None),
            P(COL, None, ROW),
        ),
        out_specs=P(COL, ROW),
        check_vma=False,
    )
```
